768 devices in a mesh: shard: 16 (over y, x_lo), replica: 48 (over z, x_hi, core).
Axes of the slice: x: 4 (x_hi: 2, x_lo: 2; x = x_hi * 2 + x_lo), y: 8, z: 12, core: 2. Of those that a mesh axis runs over, the one named last changes fastest.
Arguments:
- queries: bfloat16 [196608, 1024], P(('shard', 'replica')), may hold values from -24 to 24
- keys: bfloat16 [196608, 1024], P(('shard', 'replica')), may hold values from -6 to 6
- values: bfloat16 [196608, 1024], P(('shard', 'replica')), may hold values from -7 to 7
- positions: int32 [196608], P(('shard', 'replica')), may hold values from 0 to 255, as said below
- live: int32 [196608], P(('shard', 'replica')), may hold values from 0 to 1, as said below
- out_weight: bfloat16 [1024, 2048], P(None, 'shard'), may hold values from -0.1875 to 0.1875
- grad_out: bfloat16 [196608, 2048], P(('shard', 'replica')), may hold values from -6 to 6
Outputs:
- grad_queries: bfloat16 [196608, 1024], P(('shard', 'replica'))
- grad_keys: bfloat16 [196608, 1024], P(('shard', 'replica'))
- grad_values: bfloat16 [196608, 1024], P(('shard', 'replica'))
- grad_weight: float32 [1024, 2048], P(None, 'shard')
The draws below stay inside these ranges and needn't reach their ends.
Inputs may be any that keep to these rules, and one draw needn't show every extreme that they name: `positions`: within each aligned block of 256 tokens every grid index occurs once. Tokens of grid index under 8 are always live.
All inputs are finite; a program needn't handle non-finite values.
Results may differ from the reference program's by a relative error of at most 0.04.
Values may be sent and summed in bfloat16 or wider, within the bound.
No kernel may reach another device: no remote copies, remote signals or barrier semaphores. Data moves between devices by JAX's collectives and lax.ppermute only.
A program may use at most 64 MiB of HBM per device.

```python
import math
import jax
import jax.numpy as jnp
from jax import lax

D = 2048
HEADS = 8
HEAD_DIM = 128
PATCHES = 64
HQ = 1024
SEQ = 256
TOK_DEV = 256
TOKENS = 196608


def layout(key):
    seq_count = TOKENS // SEQ
    subkeys = jax.random.split(jax.random.fold_in(key, 11), seq_count)

    def one_perm(subkey):
        return jax.random.permutation(subkey, SEQ)
    perms = jax.vmap(one_perm)(subkeys)
    return perms.reshape(-1).astype(jnp.int32)


def draw_positions(key, part):
    return layout(key)


def draw_live(key, part):
    grid_index = layout(key)
    coin_flip = jax.random.randint(jax.random.fold_in(key, 12), (TOKENS,), 0, 4)
    return jnp.where((grid_index < 8) | (coin_flip > 0), 1, 0).astype(jnp.int32)


def base_draw(key, salt):
    return jnp.clip(jax.random.normal(jax.random.fold_in(key, salt), (TOKENS, HQ), jnp.float32), -6.0, 6.0)


def draw_queries(key, part):
    drawn = base_draw(key, 21)
    return drawn.astype(jnp.bfloat16)


def draw_keys(key, part):
    drawn = base_draw(key, 22)
    return drawn.astype(jnp.bfloat16)


def draw_values(key, part):
    drawn = jnp.clip(jax.random.normal(jax.random.fold_in(key, 31), (TOKENS, HQ), jnp.float32), -6.0, 6.0)
    return drawn.astype(jnp.bfloat16)


def shard_levels(own_key, extent, pieces, low, largest):
    def one(axis_at, shards_of):
        heights = jax.random.uniform(jax.random.fold_in(jax.random.fold_in(own_key, 6), axis_at), (shards_of,), jnp.float32, low / len(pieces), largest / len(pieces))
        return jnp.repeat(jnp.exp(heights), extent[axis_at] // shards_of).reshape((-1,) + (1,) * (len(extent) - axis_at - 1))

    loudness = one(*pieces[0])
    for cut in pieces[1:]:
        loudness = loudness * one(*cut)
    return loudness


def noise(rng, dims, scale, limit, cuts=(), kind=jnp.bfloat16):
    result = jax.random.normal(rng, dims, jnp.float32) * scale
    if len(cuts) > 0:
        result = shard_levels(rng, dims, cuts, -0.22, 0.18) * result
    return jnp.clip(result, min=-limit, max=limit).astype(kind)


def setup_inputs(seed: int = 0) -> dict:
    key_of = jax.random.split(jax.random.key(seed), 8)
    queries = draw_queries(jax.random.fold_in(key_of[7], 71), 0)
    keys = draw_keys(jax.random.fold_in(key_of[7], 71), 0)
    values = draw_values(jax.random.fold_in(key_of[7], 71), 0)
    positions = draw_positions(jax.random.fold_in(key_of[7], 71), 0)
    live = draw_live(jax.random.fold_in(key_of[7], 71), 0)
    out_weight = noise(key_of[5], (HQ, D), HQ ** -0.5, 0.1875, ((1, 16),))
    grad_out = noise(key_of[6], (TOKENS, D), 1.0, 6.0, ((0, 768),))
    return dict(queries=queries, keys=keys, values=values, positions=positions, live=live, out_weight=out_weight, grad_out=grad_out)


def attend_mask(grid_index, alive):
    frames_of = grid_index // PATCHES
    patch_of = grid_index % PATCHES
    same_frame = frames_of[:, None] == frames_of[None, :]
    earlier = (patch_of[:, None] == patch_of[None, :]) & (frames_of[None, :] < frames_of[:, None])
    itself = jnp.arange(SEQ)[:, None] == jnp.arange(SEQ)[None, :]
    return itself | (alive[None, :] == 1) & (same_frame | earlier)

def reference(queries, keys, values, positions, live, out_weight, grad_out):
    score_scale = 1.0 / math.sqrt(HEAD_DIM)
    seq_count = TOKENS // SEQ

    def one_sequence(seq_block):
        query_blk, key_blk, value_blk, grid_index, alive, grad_blk = seq_block
        grad_att = jnp.dot(grad_blk, out_weight.T, preferred_element_type=jnp.float32).astype(jnp.bfloat16)
        query_h = query_blk.reshape(SEQ, HEADS, HEAD_DIM).astype(jnp.float32)
        key_h = key_blk.reshape(SEQ, HEADS, HEAD_DIM).astype(jnp.float32)
        value_h = value_blk.reshape(SEQ, HEADS, HEAD_DIM).astype(jnp.float32)
        grad_h = grad_att.reshape(SEQ, HEADS, HEAD_DIM).astype(jnp.float32)
        allowed = attend_mask(grid_index, alive)
        scores = jnp.einsum('qhd,khd->hqk', query_h, key_h) * score_scale
        scores = jnp.where(allowed[None], scores, -jnp.inf)
        top_score = lax.optimization_barrier(jnp.max(scores, axis=-1, keepdims=True))
        expo = jnp.exp(scores - top_score)
        softmax_w = expo / lax.optimization_barrier(jnp.sum(expo, axis=-1, keepdims=True))
        probs_bf = softmax_w.astype(jnp.bfloat16)
        attended = jnp.einsum('hqk,khd->qhd', probs_bf.astype(jnp.float32), value_h).astype(jnp.bfloat16)
        grad_probs = jnp.einsum('qhd,khd->hqk', grad_h, value_h)
        row_delta = jnp.einsum('qhd,qhd->hq', grad_h, attended.astype(jnp.float32))
        scores_bf = (softmax_w * (grad_probs - row_delta[:, :, None]) * score_scale).astype(jnp.bfloat16)
        scores_f = scores_bf.astype(jnp.float32)
        grad_q = jnp.einsum('hqk,khd->qhd', scores_f, key_h).astype(jnp.bfloat16)
        grad_k = jnp.einsum('hqk,qhd->khd', scores_f, query_h).astype(jnp.bfloat16)
        grad_v = jnp.einsum('hqk,qhd->khd', probs_bf.astype(jnp.float32), grad_h).astype(jnp.bfloat16)
        return (attended.reshape(SEQ, HQ), grad_q.reshape(SEQ, HQ), grad_k.reshape(SEQ, HQ), grad_v.reshape(SEQ, HQ))
    blocks = (queries.reshape(seq_count, SEQ, HQ), keys.reshape(seq_count, SEQ, HQ), values.reshape(seq_count, SEQ, HQ), positions.reshape(seq_count, SEQ), live.reshape(seq_count, SEQ), grad_out.reshape(seq_count, SEQ, D))
    attended, grad_q, grad_k, grad_v = lax.map(one_sequence, blocks)
    devices = TOKENS // TOK_DEV
    root_tokens = math.sqrt(TOKENS)

    def add_device(running, dev_block):
        att_blk, grad_blk = dev_block
        partial_value = lax.dot_general(att_blk, grad_blk, (((0,), (0,)), ((), ())), preferred_element_type=jnp.float32)
        partial_value = (partial_value / root_tokens).astype(jnp.bfloat16)
        return (running + partial_value.astype(jnp.float32), None)
    grad_weight, ignored = lax.scan(add_device, jnp.zeros((HQ, D), jnp.float32), (attended.reshape(devices, TOK_DEV, HQ), grad_out.reshape(devices, TOK_DEV, D)))
    return (grad_q.reshape(TOKENS, HQ), grad_k.reshape(TOKENS, HQ), grad_v.reshape(TOKENS, HQ), grad_weight)
```

```python
import math

import jax
import jax.numpy as jnp
from jax import lax
from jax.sharding import PartitionSpec as P

HEADS = 8
HEAD_DIM = 128
PATCHES = 64
SEQ = 256


def local(queries, keys, values, positions, live, out_weight, grad_out):
    tok_rows = queries.shape[0]
    seq_count = tok_rows // SEQ
    q_width = out_weight.shape[0]
    score_scale = 1.0 / math.sqrt(HEAD_DIM)
    shard_count = lax.axis_size("shard")
    weight_blocks = lax.all_to_all(
        jnp.broadcast_to(out_weight[None], (shard_count,) + out_weight.shape),
        "shard",
        0,
        0,
        tiled=True,
    )
    grad_att32 = jnp.einsum(
        "tjc,jrc->tr",
        grad_out.reshape(tok_rows, shard_count, -1),
        weight_blocks,
        preferred_element_type=jnp.float32,
    )
    grad_att = grad_att32.astype(jnp.bfloat16)
    query_h = queries.reshape(seq_count, SEQ, HEADS, HEAD_DIM)
    key_h = keys.reshape(seq_count, SEQ, HEADS, HEAD_DIM)
    value_h = values.reshape(seq_count, SEQ, HEADS, HEAD_DIM)
    grad_h = grad_att.reshape(seq_count, SEQ, HEADS, HEAD_DIM)
    grid_index = positions.reshape(seq_count, SEQ)
    alive = live.reshape(seq_count, SEQ)
    frames_of = grid_index // PATCHES
    patch_of = grid_index % PATCHES
    same_frame = frames_of[:, :, None] == frames_of[:, None, :]
    earlier = (patch_of[:, :, None] == patch_of[:, None, :]) & (
        frames_of[:, None, :] < frames_of[:, :, None]
    )
    itself = (jnp.arange(SEQ)[:, None] == jnp.arange(SEQ)[None, :])[None]
    allowed = itself | (alive[:, None, :] == 1) & (same_frame | earlier)
    scores = (
        jnp.einsum("bqhd,bkhd->bhqk", query_h, key_h, preferred_element_type=jnp.float32)
        * score_scale
    )
    scores = jnp.where(allowed[:, None], scores, -jnp.inf)
    top_score = jnp.max(scores, axis=-1, keepdims=True)
    expo = jnp.exp(scores - top_score)
    softmax_w = expo / jnp.sum(expo, axis=-1, keepdims=True)
    probs_bf = softmax_w.astype(jnp.bfloat16)
    attended = jnp.einsum(
        "bhqk,bkhd->bqhd", probs_bf, value_h, preferred_element_type=jnp.float32
    ).astype(jnp.bfloat16)
    attended_rows = attended.reshape(tok_rows, q_width)
    total_tokens = tok_rows * lax.axis_size("shard") * lax.axis_size("replica")
    term = (
        jnp.einsum(
            "tr,tjc->jrc",
            attended_rows,
            grad_out.reshape(tok_rows, shard_count, -1),
            preferred_element_type=jnp.float32,
        )
        / math.sqrt(total_tokens)
    ).astype(jnp.bfloat16)
    arrived = lax.all_to_all(term, "shard", 0, 0, tiled=True)
    shard_sum = jnp.sum(arrived.astype(jnp.float32), axis=0)
    replicas = lax.axis_size("replica")
    piece_rows = -(-q_width // replicas)
    padded = jnp.pad(shard_sum, ((0, piece_rows * replicas - q_width), (0, 0)))
    pieces = lax.all_to_all(
        padded.reshape(replicas, piece_rows, -1), "replica", 0, 0, tiled=True
    )
    piece_sum = jnp.sum(pieces, axis=0)
    gathered = lax.all_to_all(
        jnp.broadcast_to(piece_sum[None], (replicas,) + piece_sum.shape),
        "replica",
        0,
        0,
        tiled=True,
    )
    grad_weight = gathered.reshape(replicas * piece_rows, -1)[:q_width]
    grad_probs = jnp.einsum("bqhd,bkhd->bhqk", grad_h, value_h, preferred_element_type=jnp.float32)
    row_delta = jnp.einsum("bqhd,bqhd->bhq", grad_h, attended, preferred_element_type=jnp.float32)
    scores_bf = (softmax_w * (grad_probs - row_delta[:, :, :, None]) * score_scale).astype(
        jnp.bfloat16
    )
    grad_q = jnp.einsum("bhqk,bkhd->bqhd", scores_bf, key_h, preferred_element_type=jnp.float32)
    grad_k = jnp.einsum("bhqk,bqhd->bkhd", scores_bf, query_h, preferred_element_type=jnp.float32)
    grad_v = jnp.einsum("bhqk,bqhd->bkhd", probs_bf, grad_h, preferred_element_type=jnp.float32)
    return (
        grad_q.astype(jnp.bfloat16).reshape(tok_rows, q_width),
        grad_k.astype(jnp.bfloat16).reshape(tok_rows, q_width),
        grad_v.astype(jnp.bfloat16).reshape(tok_rows, q_width),
        grad_weight,
    )


def solution(mesh):
    in_specs = (
        P(("shard", "replica"), None),
        P(("shard", "replica"), None),
        P(("shard", "replica"), None),
        P(("shard", "replica")),
        P(("shard", "replica")),
        P(None, "shard"),
        P(("shard", "replica"), None),
    )
    out_specs = (
        P(("shard", "replica"), None),
        P(("shard", "replica"), None),
        P(("shard", "replica"), None),
        P(None, "shard"),
    )
    return jax.shard_map(local, mesh=mesh, in_specs=in_specs, out_specs=out_specs, check_vma=False)
```

```python
import math

import jax
import jax.numpy as jnp
from jax import lax
import numpy as np
from jax.sharding import Mesh
from jax.sharding import PartitionSpec as P

HEADS = 8
HEAD_DIM = 128
PATCHES = 64
SEQ = 256


def local(queries, keys, values, positions, live, out_weight, grad_out):
    tok_rows = queries.shape[0]
    seq_count = tok_rows // SEQ
    q_width = out_weight.shape[0]
    score_scale = 1.0 / math.sqrt(HEAD_DIM)
    shard_count = lax.axis_size("shard")
    cores = lax.axis_size("core")
    core = lax.axis_index("core")
    part_rows = q_width // cores
    weight_part = lax.dynamic_slice_in_dim(out_weight, core * part_rows, part_rows, axis=0)
    weight_blocks = lax.all_to_all(
        jnp.broadcast_to(weight_part[None], (shard_count,) + weight_part.shape),
        "shard",
        0,
        0,
        tiled=True,
    )
    weight_all = lax.all_to_all(
        jnp.broadcast_to(weight_blocks[None], (cores,) + weight_blocks.shape),
        "core",
        0,
        0,
        tiled=True,
    )
    grad_att32 = jnp.einsum(
        "tjc,pjrc->tpr",
        grad_out.reshape(tok_rows, shard_count, -1),
        weight_all,
        preferred_element_type=jnp.float32,
    ).reshape(tok_rows, q_width)
    grad_att = grad_att32.astype(jnp.bfloat16)
    query_h = queries.reshape(seq_count, SEQ, HEADS, HEAD_DIM)
    key_h = keys.reshape(seq_count, SEQ, HEADS, HEAD_DIM)
    value_h = values.reshape(seq_count, SEQ, HEADS, HEAD_DIM)
    grad_h = grad_att.reshape(seq_count, SEQ, HEADS, HEAD_DIM)
    grid_index = positions.reshape(seq_count, SEQ)
    alive = live.reshape(seq_count, SEQ)
    frames_of = grid_index // PATCHES
    patch_of = grid_index % PATCHES
    same_frame = frames_of[:, :, None] == frames_of[:, None, :]
    earlier = (patch_of[:, :, None] == patch_of[:, None, :]) & (
        frames_of[:, None, :] < frames_of[:, :, None]
    )
    itself = (jnp.arange(SEQ)[:, None] == jnp.arange(SEQ)[None, :])[None]
    allowed = itself | (alive[:, None, :] == 1) & (same_frame | earlier)
    scores = (
        jnp.einsum("bqhd,bkhd->bhqk", query_h, key_h, preferred_element_type=jnp.float32)
        * score_scale
    )
    scores = jnp.where(allowed[:, None], scores, -jnp.inf)
    top_score = jnp.max(scores, axis=-1, keepdims=True)
    expo = jnp.exp(scores - top_score)
    softmax_w = expo / jnp.sum(expo, axis=-1, keepdims=True)
    probs_bf = softmax_w.astype(jnp.bfloat16)
    attended = jnp.einsum(
        "bhqk,bkhd->bqhd", probs_bf, value_h, preferred_element_type=jnp.float32
    ).astype(jnp.bfloat16)
    attended_rows = attended.reshape(tok_rows, q_width)
    total_tokens = tok_rows * lax.axis_size("shard") * lax.axis_size("rz") * lax.axis_size("core")
    term = (
        jnp.einsum(
            "tr,tjc->jrc",
            attended_rows,
            grad_out.reshape(tok_rows, shard_count, -1),
            preferred_element_type=jnp.float32,
        )
        / math.sqrt(total_tokens)
    ).astype(jnp.bfloat16)
    pair = lax.all_to_all(
        term.reshape(shard_count, cores, part_rows, -1), "core", 1, 1, tiled=True
    )
    pair_sum = jnp.sum(pair.astype(jnp.float32), axis=1).astype(jnp.bfloat16)
    arrived = lax.all_to_all(pair_sum, "shard", 0, 0, tiled=True)
    shard_sum = jnp.sum(arrived.astype(jnp.float32), axis=0)
    groups = lax.axis_size("rz")
    piece_rows = -(-part_rows // groups)
    padded = jnp.pad(shard_sum, ((0, piece_rows * groups - part_rows), (0, 0)))
    pieces = lax.all_to_all(
        padded.reshape(groups, piece_rows, -1), "rz", 0, 0, tiled=True
    )
    piece_sum = jnp.sum(pieces, axis=0)
    gathered = lax.all_to_all(
        jnp.broadcast_to(piece_sum[None], (groups * cores,) + piece_sum.shape),
        ("rz", "core"),
        0,
        0,
        tiled=True,
    )
    grad_weight = (
        gathered.reshape(groups, cores, piece_rows, -1)
        .transpose(1, 0, 2, 3)
        .reshape(cores, groups * piece_rows, -1)[:, :part_rows]
        .reshape(q_width, -1)
    )
    grad_probs = jnp.einsum("bqhd,bkhd->bhqk", grad_h, value_h, preferred_element_type=jnp.float32)
    row_delta = jnp.einsum("bqhd,bqhd->bhq", grad_h, attended, preferred_element_type=jnp.float32)
    scores_bf = (softmax_w * (grad_probs - row_delta[:, :, :, None]) * score_scale).astype(
        jnp.bfloat16
    )
    grad_q = jnp.einsum("bhqk,bkhd->bqhd", scores_bf, key_h, preferred_element_type=jnp.float32)
    grad_k = jnp.einsum("bhqk,bqhd->bkhd", scores_bf, query_h, preferred_element_type=jnp.float32)
    grad_v = jnp.einsum("bhqk,bqhd->bkhd", probs_bf, grad_h, preferred_element_type=jnp.float32)
    return (
        grad_q.astype(jnp.bfloat16).reshape(tok_rows, q_width),
        grad_k.astype(jnp.bfloat16).reshape(tok_rows, q_width),
        grad_v.astype(jnp.bfloat16).reshape(tok_rows, q_width),
        grad_weight,
    )


def solution(mesh):
    shard_size, replica_size = mesh.devices.shape
    split = Mesh(
        np.asarray(mesh.devices).reshape(shard_size, replica_size // 2, 2),
        ("shard", "rz", "core"),
    )
    rows = P(("shard", "rz", "core"), None)
    flat = P(("shard", "rz", "core"))
    in_specs = (rows, rows, rows, flat, flat, P(None, "shard"), rows)
    out_specs = (rows, rows, rows, P(None, "shard"))
    return jax.shard_map(local, mesh=split, in_specs=in_specs, out_specs=out_specs, check_vma=False)
```

```python
import math

import jax
import jax.numpy as jnp
from jax import lax
import numpy as np
from jax.sharding import Mesh
from jax.sharding import PartitionSpec as P

HEADS = 8
HEAD_DIM = 128
PATCHES = 64
SEQ = 256


def rotate(blocks, shift, axis):
    count = blocks.shape[axis]
    doubled = jnp.concatenate([blocks, blocks], axis=axis)
    return lax.dynamic_slice_in_dim(doubled, shift, count, axis=axis)


def swap_in(block, x_at):
    other = lax.ppermute(block, "xl", [(0, 1), (1, 0)])
    return jnp.where(x_at == 0, jnp.stack([block, other]), jnp.stack([other, block]))


def ring_gather(block, ys):
    right = [(i, (i + 1) % ys) for i in range(ys)]
    left = [(i, (i - 1) % ys) for i in range(ys)]
    by_offset = {0: block}
    moving = block
    for d in range(1, ys // 2 + 1):
        moving = lax.ppermute(moving, "y", right)
        by_offset[(ys - d) % ys] = moving
    moving = block
    for d in range(1, (ys - 1) // 2 + 1):
        moving = lax.ppermute(moving, "y", left)
        by_offset[d] = moving
    return jnp.stack([by_offset[o] for o in range(ys)])


def ring_reduce(blocks, ys):
    right = [(i, (i + 1) % ys) for i in range(ys)]
    left = [(i, (i - 1) % ys) for i in range(ys)]
    far_right = ys // 2
    moving = blocks[far_right]
    for d in range(far_right - 1, 0, -1):
        moving = lax.ppermute(moving, "y", right)
        moving = (moving.astype(jnp.float32) + blocks[d].astype(jnp.float32)).astype(blocks.dtype)
    from_left = lax.ppermute(moving, "y", right)
    far_left = far_right + 1
    moving = blocks[far_left]
    for d in range(far_left + 1, ys):
        moving = lax.ppermute(moving, "y", left)
        moving = (moving.astype(jnp.float32) + blocks[d].astype(jnp.float32)).astype(blocks.dtype)
    from_right = lax.ppermute(moving, "y", left)
    return (
        blocks[0].astype(jnp.float32)
        + from_left.astype(jnp.float32)
        + from_right.astype(jnp.float32)
    )


def local(queries, keys, values, positions, live, out_weight, grad_out):
    tok_rows = queries.shape[0]
    seq_count = tok_rows // SEQ
    q_width = out_weight.shape[0]
    score_scale = 1.0 / math.sqrt(HEAD_DIM)
    ys = lax.axis_size("y")
    xls = lax.axis_size("xl")
    shard_count = ys * xls
    cores = lax.axis_size("core")
    core = lax.axis_index("core")
    y_at = lax.axis_index("y")
    x_at = lax.axis_index("xl")
    part_rows = q_width // cores
    weight_part = lax.dynamic_slice_in_dim(out_weight, core * part_rows, part_rows, axis=0)
    weight_pair = swap_in(weight_part, x_at)
    weight_ring = ring_gather(weight_pair, ys)
    weight_all = lax.all_to_all(
        jnp.broadcast_to(weight_ring[None], (cores,) + weight_ring.shape),
        "core",
        0,
        0,
        tiled=True,
    )
    grad_rot = rotate(grad_out.reshape(tok_rows, ys, xls, -1), y_at, 1)
    grad_att32 = jnp.einsum(
        "toxc,poxrc->tpr",
        grad_rot,
        weight_all,
        preferred_element_type=jnp.float32,
    ).reshape(tok_rows, q_width)
    grad_att = grad_att32.astype(jnp.bfloat16)
    query_h = queries.reshape(seq_count, SEQ, HEADS, HEAD_DIM)
    key_h = keys.reshape(seq_count, SEQ, HEADS, HEAD_DIM)
    value_h = values.reshape(seq_count, SEQ, HEADS, HEAD_DIM)
    grad_h = grad_att.reshape(seq_count, SEQ, HEADS, HEAD_DIM)
    grid_index = positions.reshape(seq_count, SEQ)
    alive = live.reshape(seq_count, SEQ)
    frames_of = grid_index // PATCHES
    patch_of = grid_index % PATCHES
    same_frame = frames_of[:, :, None] == frames_of[:, None, :]
    earlier = (patch_of[:, :, None] == patch_of[:, None, :]) & (
        frames_of[:, None, :] < frames_of[:, :, None]
    )
    itself = (jnp.arange(SEQ)[:, None] == jnp.arange(SEQ)[None, :])[None]
    allowed = itself | (alive[:, None, :] == 1) & (same_frame | earlier)
    scores = (
        jnp.einsum("bqhd,bkhd->bhqk", query_h, key_h, preferred_element_type=jnp.float32)
        * score_scale
    )
    scores = jnp.where(allowed[:, None], scores, -jnp.inf)
    top_score = jnp.max(scores, axis=-1, keepdims=True)
    expo = jnp.exp(scores - top_score)
    softmax_w = expo / jnp.sum(expo, axis=-1, keepdims=True)
    probs_bf = softmax_w.astype(jnp.bfloat16)
    attended = jnp.einsum(
        "bhqk,bkhd->bqhd", probs_bf, value_h, preferred_element_type=jnp.float32
    ).astype(jnp.bfloat16)
    attended_rows = attended.reshape(tok_rows, q_width)
    total_tokens = tok_rows * lax.axis_size("y") * lax.axis_size("xl") * lax.axis_size("rz") * lax.axis_size("core")
    term = (
        jnp.einsum(
            "tr,tjc->jrc",
            attended_rows,
            grad_out.reshape(tok_rows, shard_count, -1),
            preferred_element_type=jnp.float32,
        )
        / math.sqrt(total_tokens)
    ).astype(jnp.bfloat16)
    pair = lax.all_to_all(
        term.reshape(shard_count, cores, part_rows, -1), "core", 1, 1, tiled=True
    )
    pair_sum = jnp.sum(pair.astype(jnp.float32), axis=1).astype(jnp.bfloat16)
    pair_rot = rotate(pair_sum.reshape(ys, xls, part_rows, -1), y_at, 0)
    y_sum = ring_reduce(pair_rot, ys)
    keep = jnp.where(x_at == 0, y_sum[0], y_sum[1])
    send = jnp.where(x_at == 0, y_sum[1], y_sum[0])
    shard_sum = keep + lax.ppermute(send, "xl", [(0, 1), (1, 0)])
    groups = lax.axis_size("rz")
    piece_rows = -(-part_rows // groups)
    padded = jnp.pad(shard_sum, ((0, piece_rows * groups - part_rows), (0, 0)))
    pieces = lax.all_to_all(
        padded.reshape(groups, piece_rows, -1), "rz", 0, 0, tiled=True
    )
    piece_sum = jnp.sum(pieces, axis=0)
    gathered = lax.all_to_all(
        jnp.broadcast_to(piece_sum[None], (groups * cores,) + piece_sum.shape),
        ("rz", "core"),
        0,
        0,
        tiled=True,
    )
    grad_weight = (
        gathered.reshape(groups, cores, piece_rows, -1)
        .transpose(1, 0, 2, 3)
        .reshape(cores, groups * piece_rows, -1)[:, :part_rows]
        .reshape(q_width, -1)
    )
    grad_probs = jnp.einsum("bqhd,bkhd->bhqk", grad_h, value_h, preferred_element_type=jnp.float32)
    row_delta = jnp.einsum("bqhd,bqhd->bhq", grad_h, attended, preferred_element_type=jnp.float32)
    scores_bf = (softmax_w * (grad_probs - row_delta[:, :, :, None]) * score_scale).astype(
        jnp.bfloat16
    )
    grad_q = jnp.einsum("bhqk,bkhd->bqhd", scores_bf, key_h, preferred_element_type=jnp.float32)
    grad_k = jnp.einsum("bhqk,bqhd->bkhd", scores_bf, query_h, preferred_element_type=jnp.float32)
    grad_v = jnp.einsum("bhqk,bqhd->bkhd", probs_bf, grad_h, preferred_element_type=jnp.float32)
    return (
        grad_q.astype(jnp.bfloat16).reshape(tok_rows, q_width),
        grad_k.astype(jnp.bfloat16).reshape(tok_rows, q_width),
        grad_v.astype(jnp.bfloat16).reshape(tok_rows, q_width),
        grad_weight,
    )


def solution(mesh):
    shard_size, replica_size = mesh.devices.shape
    split = Mesh(
        np.asarray(mesh.devices).reshape(shard_size // 2, 2, replica_size // 2, 2),
        ("y", "xl", "rz", "core"),
    )
    rows = P(("y", "xl", "rz", "core"), None)
    flat = P(("y", "xl", "rz", "core"))
    columns = P(None, ("y", "xl"))
    in_specs = (rows, rows, rows, flat, flat, columns, rows)
    out_specs = (rows, rows, rows, columns)
    return jax.shard_map(local, mesh=split, in_specs=in_specs, out_specs=out_specs, check_vma=False)
```

```python
import math

import jax
import jax.numpy as jnp
from jax import lax
import numpy as np
from jax.sharding import Mesh
from jax.sharding import PartitionSpec as P

HEADS = 8
HEAD_DIM = 128
PATCHES = 64
SEQ = 256


def rotate(blocks, shift, axis):
    count = blocks.shape[axis]
    doubled = jnp.concatenate([blocks, blocks], axis=axis)
    return lax.dynamic_slice_in_dim(doubled, shift, count, axis=axis)


def swap_in(block, x_at):
    other = lax.ppermute(block, "xl", [(0, 1), (1, 0)])
    return jnp.where(x_at == 0, jnp.stack([block, other]), jnp.stack([other, block]))


def ring_gather(block, ys):
    right = [(i, (i + 1) % ys) for i in range(ys)]
    left = [(i, (i - 1) % ys) for i in range(ys)]
    by_offset = {0: block}
    moving = block
    for d in range(1, ys // 2 + 1):
        moving = lax.ppermute(moving, "y", right)
        by_offset[(ys - d) % ys] = moving
    moving = block
    for d in range(1, (ys - 1) // 2 + 1):
        moving = lax.ppermute(moving, "y", left)
        by_offset[d] = moving
    return jnp.stack([by_offset[o] for o in range(ys)])


def ring_reduce(blocks, ys):
    right = [(i, (i + 1) % ys) for i in range(ys)]
    left = [(i, (i - 1) % ys) for i in range(ys)]
    far_right = ys // 2
    moving = blocks[far_right]
    for d in range(far_right - 1, 0, -1):
        moving = lax.ppermute(moving, "y", right)
        moving = (moving.astype(jnp.float32) + blocks[d].astype(jnp.float32)).astype(blocks.dtype)
    from_left = lax.ppermute(moving, "y", right)
    far_left = far_right + 1
    moving = blocks[far_left]
    for d in range(far_left + 1, ys):
        moving = lax.ppermute(moving, "y", left)
        moving = (moving.astype(jnp.float32) + blocks[d].astype(jnp.float32)).astype(blocks.dtype)
    from_right = lax.ppermute(moving, "y", left)
    return (
        blocks[0].astype(jnp.float32)
        + from_left.astype(jnp.float32)
        + from_right.astype(jnp.float32)
    )


def local(queries, keys, values, positions, live, out_weight, grad_out):
    tok_rows = queries.shape[0]
    seq_count = tok_rows // SEQ
    q_width = out_weight.shape[0]
    score_scale = 1.0 / math.sqrt(HEAD_DIM)
    ys = lax.axis_size("y")
    xls = lax.axis_size("xl")
    shard_count = ys * xls
    cores = lax.axis_size("core")
    core = lax.axis_index("core")
    y_at = lax.axis_index("y")
    x_at = lax.axis_index("xl")
    part_rows = q_width // cores
    weight_part = lax.dynamic_slice_in_dim(out_weight, core * part_rows, part_rows, axis=0)
    weight_pair = swap_in(weight_part, x_at)
    query_h = queries.reshape(seq_count, SEQ, HEADS, HEAD_DIM)
    key_h = keys.reshape(seq_count, SEQ, HEADS, HEAD_DIM)
    value_h = values.reshape(seq_count, SEQ, HEADS, HEAD_DIM)
    grid_index = positions.reshape(seq_count, SEQ)
    alive = live.reshape(seq_count, SEQ)
    frames_of = grid_index // PATCHES
    patch_of = grid_index % PATCHES
    same_frame = frames_of[:, :, None] == frames_of[:, None, :]
    earlier = (patch_of[:, :, None] == patch_of[:, None, :]) & (
        frames_of[:, None, :] < frames_of[:, :, None]
    )
    itself = (jnp.arange(SEQ)[:, None] == jnp.arange(SEQ)[None, :])[None]
    allowed = itself | (alive[:, None, :] == 1) & (same_frame | earlier)
    scores = (
        jnp.einsum("bqhd,bkhd->bhqk", query_h, key_h, preferred_element_type=jnp.float32)
        * score_scale
    )
    scores = jnp.where(allowed[:, None], scores, -jnp.inf)
    top_score = jnp.max(scores, axis=-1, keepdims=True)
    expo = jnp.exp(scores - top_score)
    softmax_w = expo / jnp.sum(expo, axis=-1, keepdims=True)
    probs_bf = softmax_w.astype(jnp.bfloat16)
    attended = jnp.einsum(
        "bhqk,bkhd->bqhd", probs_bf, value_h, preferred_element_type=jnp.float32
    ).astype(jnp.bfloat16)
    attended_rows = attended.reshape(tok_rows, q_width)
    total_tokens = tok_rows * lax.axis_size("y") * lax.axis_size("xl") * lax.axis_size("rz") * lax.axis_size("core")
    term = (
        jnp.einsum(
            "tr,tjc->jrc",
            attended_rows,
            grad_out.reshape(tok_rows, shard_count, -1),
            preferred_element_type=jnp.float32,
        )
        / math.sqrt(total_tokens)
    ).astype(jnp.bfloat16)
    pair = lax.all_to_all(
        term.reshape(shard_count, cores, part_rows, -1), "core", 1, 1, tiled=True
    )
    pair_sum = jnp.sum(pair.astype(jnp.float32), axis=1).astype(jnp.bfloat16)
    pair_rot = rotate(pair_sum.reshape(ys, xls, part_rows, -1), y_at, 0)
    weight_pair, pair_rot = lax.optimization_barrier((weight_pair, pair_rot))
    weight_ring = ring_gather(weight_pair, ys)
    weight_all = lax.all_to_all(
        jnp.broadcast_to(weight_ring[None], (cores,) + weight_ring.shape),
        "core",
        0,
        0,
        tiled=True,
    )
    grad_rot = rotate(grad_out.reshape(tok_rows, ys, xls, -1), y_at, 1)
    grad_att32 = jnp.einsum(
        "toxc,poxrc->tpr",
        grad_rot,
        weight_all,
        preferred_element_type=jnp.float32,
    ).reshape(tok_rows, q_width)
    grad_att = grad_att32.astype(jnp.bfloat16)
    grad_h = grad_att.reshape(seq_count, SEQ, HEADS, HEAD_DIM)
    y_sum = ring_reduce(pair_rot, ys)
    keep = jnp.where(x_at == 0, y_sum[0], y_sum[1])
    send = jnp.where(x_at == 0, y_sum[1], y_sum[0])
    shard_sum = keep + lax.ppermute(send, "xl", [(0, 1), (1, 0)])
    groups = lax.axis_size("rz")
    piece_rows = -(-part_rows // groups)
    padded = jnp.pad(shard_sum, ((0, piece_rows * groups - part_rows), (0, 0)))
    pieces = lax.all_to_all(
        padded.reshape(groups, piece_rows, -1), "rz", 0, 0, tiled=True
    )
    piece_sum = jnp.sum(pieces, axis=0)
    gathered = lax.all_to_all(
        jnp.broadcast_to(piece_sum[None], (groups * cores,) + piece_sum.shape),
        ("rz", "core"),
        0,
        0,
        tiled=True,
    )
    grad_weight = (
        gathered.reshape(groups, cores, piece_rows, -1)
        .transpose(1, 0, 2, 3)
        .reshape(cores, groups * piece_rows, -1)[:, :part_rows]
        .reshape(q_width, -1)
    )
    grad_probs = jnp.einsum("bqhd,bkhd->bhqk", grad_h, value_h, preferred_element_type=jnp.float32)
    row_delta = jnp.einsum("bqhd,bqhd->bhq", grad_h, attended, preferred_element_type=jnp.float32)
    scores_bf = (softmax_w * (grad_probs - row_delta[:, :, :, None]) * score_scale).astype(
        jnp.bfloat16
    )
    grad_q = jnp.einsum("bhqk,bkhd->bqhd", scores_bf, key_h, preferred_element_type=jnp.float32)
    grad_k = jnp.einsum("bhqk,bqhd->bkhd", scores_bf, query_h, preferred_element_type=jnp.float32)
    grad_v = jnp.einsum("bhqk,bqhd->bkhd", probs_bf, grad_h, preferred_element_type=jnp.float32)
    return (
        grad_q.astype(jnp.bfloat16).reshape(tok_rows, q_width),
        grad_k.astype(jnp.bfloat16).reshape(tok_rows, q_width),
        grad_v.astype(jnp.bfloat16).reshape(tok_rows, q_width),
        grad_weight,
    )


def solution(mesh):
    shard_size, replica_size = mesh.devices.shape
    split = Mesh(
        np.asarray(mesh.devices).reshape(shard_size // 2, 2, replica_size // 2, 2),
        ("y", "xl", "rz", "core"),
    )
    rows = P(("y", "xl", "rz", "core"), None)
    flat = P(("y", "xl", "rz", "core"))
    columns = P(None, ("y", "xl"))
    in_specs = (rows, rows, rows, flat, flat, columns, rows)
    out_specs = (rows, rows, rows, columns)
    return jax.shard_map(local, mesh=split, in_specs=in_specs, out_specs=out_specs, check_vma=False)
```

```python
import math

import jax
import jax.numpy as jnp
from jax import lax
import numpy as np
from jax.sharding import Mesh
from jax.sharding import PartitionSpec as P

HEADS = 8
HEAD_DIM = 128
PATCHES = 64
SEQ = 256


def rotate(blocks, shift, axis):
    count = blocks.shape[axis]
    doubled = jnp.concatenate([blocks, blocks], axis=axis)
    return lax.dynamic_slice_in_dim(doubled, shift, count, axis=axis)


def swap_in(block, x_at):
    other = lax.ppermute(block, "xl", [(0, 1), (1, 0)])
    return jnp.where(x_at == 0, jnp.stack([block, other]), jnp.stack([other, block]))


def ring_gather(block, ys):
    right = [(i, (i + 1) % ys) for i in range(ys)]
    left = [(i, (i - 1) % ys) for i in range(ys)]
    by_offset = {0: block}
    moving = block
    for d in range(1, ys // 2 + 1):
        moving = lax.ppermute(moving, "y", right)
        by_offset[(ys - d) % ys] = moving
    moving = block
    for d in range(1, (ys - 1) // 2 + 1):
        moving = lax.ppermute(moving, "y", left)
        by_offset[d] = moving
    return jnp.stack([by_offset[o] for o in range(ys)])


def ring_reduce(blocks, ys):
    right = [(i, (i + 1) % ys) for i in range(ys)]
    left = [(i, (i - 1) % ys) for i in range(ys)]
    far_right = ys // 2
    moving = blocks[far_right]
    for d in range(far_right - 1, 0, -1):
        moving = lax.ppermute(moving, "y", right)
        moving = (moving.astype(jnp.float32) + blocks[d].astype(jnp.float32)).astype(blocks.dtype)
    from_left = lax.ppermute(moving, "y", right)
    far_left = far_right + 1
    moving = blocks[far_left]
    for d in range(far_left + 1, ys):
        moving = lax.ppermute(moving, "y", left)
        moving = (moving.astype(jnp.float32) + blocks[d].astype(jnp.float32)).astype(blocks.dtype)
    from_right = lax.ppermute(moving, "y", left)
    return (
        blocks[0].astype(jnp.float32)
        + from_left.astype(jnp.float32)
        + from_right.astype(jnp.float32)
    )


def local(queries, keys, values, positions, live, out_weight, grad_out):
    tok_rows = queries.shape[0]
    seq_count = tok_rows // SEQ
    q_width = out_weight.shape[0]
    score_scale = 1.0 / math.sqrt(HEAD_DIM)
    ys = lax.axis_size("y")
    xls = lax.axis_size("xl")
    shard_count = ys * xls
    cores = lax.axis_size("core")
    core = lax.axis_index("core")
    y_at = lax.axis_index("y")
    x_at = lax.axis_index("xl")
    part_rows = q_width // cores
    weight_part = lax.dynamic_slice_in_dim(out_weight, core * part_rows, part_rows, axis=0)
    weight_pair = swap_in(weight_part, x_at)
    query_h = queries.reshape(seq_count, SEQ, HEADS, HEAD_DIM)
    key_h = keys.reshape(seq_count, SEQ, HEADS, HEAD_DIM)
    value_h = values.reshape(seq_count, SEQ, HEADS, HEAD_DIM)
    grid_index = positions.reshape(seq_count, SEQ)
    alive = live.reshape(seq_count, SEQ)
    frames_of = grid_index // PATCHES
    patch_of = grid_index % PATCHES
    same_frame = frames_of[:, :, None] == frames_of[:, None, :]
    earlier = (patch_of[:, :, None] == patch_of[:, None, :]) & (
        frames_of[:, None, :] < frames_of[:, :, None]
    )
    itself = (jnp.arange(SEQ)[:, None] == jnp.arange(SEQ)[None, :])[None]
    allowed = itself | (alive[:, None, :] == 1) & (same_frame | earlier)
    scores = (
        jnp.einsum("bqhd,bkhd->bhqk", query_h, key_h, preferred_element_type=jnp.float32)
        * score_scale
    )
    scores = jnp.where(allowed[:, None], scores, -jnp.inf)
    top_score = jnp.max(scores, axis=-1, keepdims=True)
    expo = jnp.exp(scores - top_score)
    softmax_w = expo / jnp.sum(expo, axis=-1, keepdims=True)
    probs_bf = softmax_w.astype(jnp.bfloat16)
    attended = jnp.einsum(
        "bhqk,bkhd->bqhd", probs_bf, value_h, preferred_element_type=jnp.float32
    ).astype(jnp.bfloat16)
    attended_rows = attended.reshape(tok_rows, q_width)
    total_tokens = tok_rows * lax.axis_size("y") * lax.axis_size("xl") * lax.axis_size("rz") * lax.axis_size("core")
    term = (
        jnp.einsum(
            "tr,tjc->jrc",
            attended_rows,
            grad_out.reshape(tok_rows, shard_count, -1),
            preferred_element_type=jnp.float32,
        )
        / math.sqrt(total_tokens)
    ).astype(jnp.bfloat16)
    halves = term.reshape(shard_count, cores, part_rows, -1)
    own_half = jnp.where(core == 0, halves[:, 0], halves[:, 1])
    sent_half = jnp.where(core == 0, halves[:, 1], halves[:, 0])
    got_half = lax.ppermute(sent_half, "core", [(0, 1), (1, 0)])
    pair_sum = (own_half.astype(jnp.float32) + got_half.astype(jnp.float32)).astype(jnp.bfloat16)
    pair_rot = rotate(pair_sum.reshape(ys, xls, part_rows, -1), y_at, 0)
    weight_pair, pair_rot = lax.optimization_barrier((weight_pair, pair_rot))
    weight_ring = ring_gather(weight_pair, ys)
    weight_other = lax.ppermute(weight_ring, "core", [(0, 1), (1, 0)])
    grad_rot = rotate(grad_out.reshape(tok_rows, ys, xls, -1), y_at, 1)
    own_cols = jnp.einsum(
        "toxc,oxrc->tr", grad_rot, weight_ring, preferred_element_type=jnp.float32
    )
    other_cols = jnp.einsum(
        "toxc,oxrc->tr", grad_rot, weight_other, preferred_element_type=jnp.float32
    )
    grad_att32 = jnp.where(
        core == 0,
        jnp.concatenate([own_cols, other_cols], axis=1),
        jnp.concatenate([other_cols, own_cols], axis=1),
    )
    grad_att = grad_att32.astype(jnp.bfloat16)
    grad_h = grad_att.reshape(seq_count, SEQ, HEADS, HEAD_DIM)
    y_sum = ring_reduce(pair_rot, ys)
    keep = jnp.where(x_at == 0, y_sum[0], y_sum[1])
    send = jnp.where(x_at == 0, y_sum[1], y_sum[0])
    shard_sum = keep + lax.ppermute(send, "xl", [(0, 1), (1, 0)])
    groups = lax.axis_size("rz")
    piece_rows = -(-part_rows // groups)
    padded = jnp.pad(shard_sum, ((0, piece_rows * groups - part_rows), (0, 0)))
    pieces = lax.all_to_all(
        padded.reshape(groups, piece_rows, -1), "rz", 0, 0, tiled=True
    )
    piece_sum = jnp.sum(pieces, axis=0)
    gathered = lax.all_to_all(
        jnp.broadcast_to(piece_sum[None], (groups * cores,) + piece_sum.shape),
        ("rz", "core"),
        0,
        0,
        tiled=True,
    )
    grad_weight = (
        gathered.reshape(groups, cores, piece_rows, -1)
        .transpose(1, 0, 2, 3)
        .reshape(cores, groups * piece_rows, -1)[:, :part_rows]
        .reshape(q_width, -1)
    )
    grad_probs = jnp.einsum("bqhd,bkhd->bhqk", grad_h, value_h, preferred_element_type=jnp.float32)
    row_delta = jnp.einsum("bqhd,bqhd->bhq", grad_h, attended, preferred_element_type=jnp.float32)
    scores_bf = (softmax_w * (grad_probs - row_delta[:, :, :, None]) * score_scale).astype(
        jnp.bfloat16
    )
    grad_q = jnp.einsum("bhqk,bkhd->bqhd", scores_bf, key_h, preferred_element_type=jnp.float32)
    grad_k = jnp.einsum("bhqk,bqhd->bkhd", scores_bf, query_h, preferred_element_type=jnp.float32)
    grad_v = jnp.einsum("bhqk,bqhd->bkhd", probs_bf, grad_h, preferred_element_type=jnp.float32)
    return (
        grad_q.astype(jnp.bfloat16).reshape(tok_rows, q_width),
        grad_k.astype(jnp.bfloat16).reshape(tok_rows, q_width),
        grad_v.astype(jnp.bfloat16).reshape(tok_rows, q_width),
        grad_weight,
    )


def solution(mesh):
    shard_size, replica_size = mesh.devices.shape
    split = Mesh(
        np.asarray(mesh.devices).reshape(shard_size // 2, 2, replica_size // 2, 2),
        ("y", "xl", "rz", "core"),
    )
    rows = P(("y", "xl", "rz", "core"), None)
    flat = P(("y", "xl", "rz", "core"))
    columns = P(None, ("y", "xl"))
    in_specs = (rows, rows, rows, flat, flat, columns, rows)
    out_specs = (rows, rows, rows, columns)
    return jax.shard_map(local, mesh=split, in_specs=in_specs, out_specs=out_specs, check_vma=False)
```

```python
import math

import jax
import jax.numpy as jnp
from jax import lax
import numpy as np
from jax.sharding import Mesh
from jax.sharding import PartitionSpec as P

HEADS = 8
HEAD_DIM = 128
PATCHES = 64
SEQ = 256


def rotate(blocks, shift, axis):
    count = blocks.shape[axis]
    doubled = jnp.concatenate([blocks, blocks], axis=axis)
    return lax.dynamic_slice_in_dim(doubled, shift, count, axis=axis)


def swap_in(block, x_at):
    other = lax.ppermute(block, "xl", [(0, 1), (1, 0)])
    return jnp.where(x_at == 0, jnp.stack([block, other]), jnp.stack([other, block]))


def ring_gather(block, ys):
    right = [(i, (i + 1) % ys) for i in range(ys)]
    left = [(i, (i - 1) % ys) for i in range(ys)]
    by_offset = {0: block}
    moving = block
    for d in range(1, ys // 2 + 1):
        moving = lax.ppermute(moving, "y", right)
        by_offset[(ys - d) % ys] = moving
    moving = block
    for d in range(1, (ys - 1) // 2 + 1):
        moving = lax.ppermute(moving, "y", left)
        by_offset[d] = moving
    return jnp.stack([by_offset[o] for o in range(ys)])


def ring_reduce(blocks, ys):
    right = [(i, (i + 1) % ys) for i in range(ys)]
    left = [(i, (i - 1) % ys) for i in range(ys)]
    far_right = ys // 2
    moving = blocks[far_right]
    for d in range(far_right - 1, 0, -1):
        moving = lax.ppermute(moving, "y", right)
        moving = (moving.astype(jnp.float32) + blocks[d].astype(jnp.float32)).astype(blocks.dtype)
    from_left = lax.ppermute(moving, "y", right)
    far_left = far_right + 1
    moving = blocks[far_left]
    for d in range(far_left + 1, ys):
        moving = lax.ppermute(moving, "y", left)
        moving = (moving.astype(jnp.float32) + blocks[d].astype(jnp.float32)).astype(blocks.dtype)
    from_right = lax.ppermute(moving, "y", left)
    return (
        blocks[0].astype(jnp.float32)
        + from_left.astype(jnp.float32)
        + from_right.astype(jnp.float32)
    )


def local(queries, keys, values, positions, live, out_weight, grad_out):
    tok_rows = queries.shape[0]
    seq_count = tok_rows // SEQ
    q_width = out_weight.shape[0]
    score_scale = 1.0 / math.sqrt(HEAD_DIM)
    ys = lax.axis_size("y")
    xls = lax.axis_size("xl")
    shard_count = ys * xls
    cores = lax.axis_size("core")
    core = lax.axis_index("core")
    y_at = lax.axis_index("y")
    x_at = lax.axis_index("xl")
    part_rows = q_width // cores
    weight_part = lax.dynamic_slice_in_dim(out_weight, core * part_rows, part_rows, axis=0)
    weight_pair = swap_in(weight_part, x_at)
    query_h = queries.reshape(seq_count, SEQ, HEADS, HEAD_DIM)
    key_h = keys.reshape(seq_count, SEQ, HEADS, HEAD_DIM)
    value_h = values.reshape(seq_count, SEQ, HEADS, HEAD_DIM)
    grid_index = positions.reshape(seq_count, SEQ)
    alive = live.reshape(seq_count, SEQ)
    frames_of = grid_index // PATCHES
    patch_of = grid_index % PATCHES
    same_frame = frames_of[:, :, None] == frames_of[:, None, :]
    earlier = (patch_of[:, :, None] == patch_of[:, None, :]) & (
        frames_of[:, None, :] < frames_of[:, :, None]
    )
    itself = (jnp.arange(SEQ)[:, None] == jnp.arange(SEQ)[None, :])[None]
    allowed = itself | (alive[:, None, :] == 1) & (same_frame | earlier)
    scores = (
        jnp.einsum("bqhd,bkhd->bhqk", query_h, key_h, preferred_element_type=jnp.float32)
        * score_scale
    )
    scores = jnp.where(allowed[:, None], scores, -jnp.inf)
    top_score = jnp.max(scores, axis=-1, keepdims=True)
    expo = jnp.exp(scores - top_score)
    softmax_w = expo / jnp.sum(expo, axis=-1, keepdims=True)
    probs_bf = softmax_w.astype(jnp.bfloat16)
    attended = jnp.einsum(
        "bhqk,bkhd->bqhd", probs_bf, value_h, preferred_element_type=jnp.float32
    ).astype(jnp.bfloat16)
    attended_rows = attended.reshape(tok_rows, q_width)
    total_tokens = tok_rows * lax.axis_size("y") * lax.axis_size("xl") * lax.axis_size("rz") * lax.axis_size("core")
    term = (
        jnp.einsum(
            "tr,tjc->jrc",
            attended_rows,
            grad_out.reshape(tok_rows, shard_count, -1),
            preferred_element_type=jnp.float32,
        )
        / math.sqrt(total_tokens)
    ).astype(jnp.bfloat16)
    halves = term.reshape(shard_count, cores, part_rows, -1)
    own_half = jnp.where(core == 0, halves[:, 0], halves[:, 1])
    sent_half = jnp.where(core == 0, halves[:, 1], halves[:, 0])
    got_half = lax.ppermute(sent_half, "core", [(0, 1), (1, 0)])
    pair_sum = (own_half.astype(jnp.float32) + got_half.astype(jnp.float32)).astype(jnp.bfloat16)
    pair_rot = rotate(pair_sum.reshape(ys, xls, part_rows, -1), y_at, 0)
    weight_pair, pair_rot = lax.optimization_barrier((weight_pair, pair_rot))
    weight_ring = ring_gather(weight_pair, ys)
    weight_other = lax.ppermute(weight_ring, "core", [(0, 1), (1, 0)])
    grad_rot = rotate(grad_out.reshape(tok_rows, ys, xls, -1), y_at, 1)
    own_cols = jnp.einsum(
        "toxc,oxrc->tr", grad_rot, weight_ring, preferred_element_type=jnp.float32
    )
    other_cols = jnp.einsum(
        "toxc,oxrc->tr", grad_rot, weight_other, preferred_element_type=jnp.float32
    )
    grad_att32 = jnp.where(
        core == 0,
        jnp.concatenate([own_cols, other_cols], axis=1),
        jnp.concatenate([other_cols, own_cols], axis=1),
    )
    grad_att = grad_att32.astype(jnp.bfloat16)
    grad_h = grad_att.reshape(seq_count, SEQ, HEADS, HEAD_DIM)
    y_sum = ring_reduce(pair_rot, ys)
    keep = jnp.where(x_at == 0, y_sum[0], y_sum[1])
    send = jnp.where(x_at == 0, y_sum[1], y_sum[0])
    shard_sum = keep + lax.ppermute(send, "xl", [(0, 1), (1, 0)])
    groups = lax.axis_size("rz")
    piece_rows = -(-part_rows // groups)
    padded = jnp.pad(shard_sum, ((0, piece_rows * groups - part_rows), (0, 0)))
    padded, grad_att = lax.optimization_barrier((padded, grad_att))
    grad_h = grad_att.reshape(seq_count, SEQ, HEADS, HEAD_DIM)
    pieces = lax.all_to_all(
        padded.reshape(groups, piece_rows, -1), "rz", 0, 0, tiled=True
    )
    piece_sum = jnp.sum(pieces, axis=0)
    gathered = lax.all_to_all(
        jnp.broadcast_to(piece_sum[None], (groups * cores,) + piece_sum.shape),
        ("rz", "core"),
        0,
        0,
        tiled=True,
    )
    grad_weight = (
        gathered.reshape(groups, cores, piece_rows, -1)
        .transpose(1, 0, 2, 3)
        .reshape(cores, groups * piece_rows, -1)[:, :part_rows]
        .reshape(q_width, -1)
    )
    grad_probs = jnp.einsum("bqhd,bkhd->bhqk", grad_h, value_h, preferred_element_type=jnp.float32)
    row_delta = jnp.einsum("bqhd,bqhd->bhq", grad_h, attended, preferred_element_type=jnp.float32)
    scores_bf = (softmax_w * (grad_probs - row_delta[:, :, :, None]) * score_scale).astype(
        jnp.bfloat16
    )
    grad_q = jnp.einsum("bhqk,bkhd->bqhd", scores_bf, key_h, preferred_element_type=jnp.float32)
    grad_k = jnp.einsum("bhqk,bqhd->bkhd", scores_bf, query_h, preferred_element_type=jnp.float32)
    grad_v = jnp.einsum("bhqk,bqhd->bkhd", probs_bf, grad_h, preferred_element_type=jnp.float32)
    return (
        grad_q.astype(jnp.bfloat16).reshape(tok_rows, q_width),
        grad_k.astype(jnp.bfloat16).reshape(tok_rows, q_width),
        grad_v.astype(jnp.bfloat16).reshape(tok_rows, q_width),
        grad_weight,
    )


def solution(mesh):
    shard_size, replica_size = mesh.devices.shape
    split = Mesh(
        np.asarray(mesh.devices).reshape(shard_size // 2, 2, replica_size // 2, 2),
        ("y", "xl", "rz", "core"),
    )
    rows = P(("y", "xl", "rz", "core"), None)
    flat = P(("y", "xl", "rz", "core"))
    columns = P(None, ("y", "xl"))
    in_specs = (rows, rows, rows, flat, flat, columns, rows)
    out_specs = (rows, rows, rows, columns)
    return jax.shard_map(local, mesh=split, in_specs=in_specs, out_specs=out_specs, check_vma=False)
```
